512 devices in a mesh: dp: 32 (over x, y), expert: 16 (over z, core).
Axes of the slice: x: 4, y: 8, z: 8, core: 2. Of those that a mesh axis runs over, the one named last changes fastest.
Arguments:
- tokens: bfloat16 [65536, 2048], P(('dp', 'expert')), may hold values from -6 to 6
- cotangent: bfloat16 [65536, 2048], P(('dp', 'expert')), may hold values from -6 to 6
- expert_ids: int32 [65536, 2], P(('dp', 'expert')), may hold values from 0 to 15, as said below
- router_probs: float32 [65536, 2], P(('dp', 'expert')), may hold values from 0.1 to 1
- gate_weight: bfloat16 [16, 2048, 768], P('expert', 'dp'), may hold values from -0.125 to 0.125
- up_weight: bfloat16 [16, 2048, 768], P('expert', 'dp'), may hold values from -0.125 to 0.125
- down_weight: bfloat16 [16, 768, 2048], P('expert', 'dp'), may hold values from -0.21875 to 0.21875
Outputs:
- mixed_out: bfloat16 [65536, 2048], P(('dp', 'expert'))
- grad_tokens: bfloat16 [65536, 2048], P(('dp', 'expert'))
- grad_probs: float32 [65536, 2], P(('dp', 'expert'))
- grad_down: bfloat16 [16, 768, 2048], P('expert', 'dp')
The draws below stay inside these ranges and needn't reach their ends.
Inputs may be any that keep to these rules, and one draw needn't show every extreme that they name: `expert_ids`: each token names 2 different experts. In each aligned block of 128 tokens (the tokens of one device) no expert is named more than 18 times, and in each aligned group of 16 such blocks one expert is named exactly 18 times in every block of the group.
All inputs are finite; a program needn't handle non-finite values.
Results may differ from the reference program's by a relative error of at most 0.023.
Values may be sent and summed in bfloat16 or wider, within the bound.
No kernel may reach another device: no remote copies, remote signals or barrier semaphores. Data moves between devices by JAX's collectives and lax.ppermute only.
A program may use at most 64 MiB of HBM per device.

```python
import math
import jax
import jax.numpy as jnp
from jax import lax

D = 2048
H = 768
K = 2
TOK_DEV = 128
EXPERTS = 16
CAP = 18
TOKENS = 65536
N_DP = 32


def draw_block(block_key, hot_expert):
    seat_key, order_key = jax.random.split(block_key)
    slot_total = TOK_DEV * K
    spare = slot_total - CAP
    seats = jax.random.permutation(seat_key, (EXPERTS - 1) * CAP)[:spare] // CAP
    owners = seats + (seats >= hot_expert).astype(jnp.int32)
    experts_range = jnp.arange(EXPERTS, dtype=jnp.int32)
    counts = jnp.sum((owners[None, :] == experts_range[:, None]).astype(jnp.int32), axis=1)
    counts = counts + CAP * (experts_range == hot_expert).astype(jnp.int32)
    ends = jnp.cumsum(counts)
    slot_range = jnp.arange(slot_total, dtype=jnp.int32)
    sorted_ids = jnp.sum((ends[None, :] <= slot_range[:, None]).astype(jnp.int32), axis=1)
    table = sorted_ids.reshape(K, TOK_DEV).T
    order = jax.random.permutation(order_key, TOK_DEV)
    return table[order].astype(jnp.int32)


def draw_expert_ids(key, part):
    block_count = TOKENS // TOK_DEV
    group_count = block_count // EXPERTS
    hot_list = jax.random.randint(jax.random.fold_in(key, 7), (group_count,), 0, EXPERTS).astype(jnp.int32)
    hot_blocks = jnp.repeat(hot_list, EXPERTS)
    block_keys = jax.random.split(jax.random.fold_in(key, 11), block_count)
    return jax.vmap(draw_block)(block_keys, hot_blocks).reshape(TOKENS, K)


def shard_levels(key, shape, cuts, smallest, largest):
    def one(axis_at, shards_of):
        draws = jax.random.uniform(jax.random.fold_in(jax.random.fold_in(key, 6), axis_at), (shards_of,), jnp.float32, smallest / len(cuts), largest / len(cuts))
        return jnp.repeat(jnp.exp(draws), shape[axis_at] // shards_of).reshape((-1,) + (1,) * (len(shape) - axis_at - 1))

    loudness = one(*cuts[0])
    for cut in cuts[1:]:
        loudness = loudness * one(*cut)
    return loudness


def gaussian(key, extent, spread, most, shards=(), held_as=jnp.bfloat16):
    entries = jax.random.normal(key, extent, jnp.float32) * spread
    if len(shards) > 0:
        entries = shard_levels(key, extent, shards, -0.22, 0.18) * entries
    return jnp.clip(entries, min=-most, max=most).astype(held_as)


def setup_inputs(seed: int = 0) -> dict:
    arg_keys = jax.random.split(jax.random.key(seed), 8)
    tokens = gaussian(arg_keys[0], (TOKENS, D), 1.0, 6.0, ((0, 512),))
    cotangent = gaussian(arg_keys[1], (TOKENS, D), 1.0, 6.0, ((0, 512),))
    expert_ids = draw_expert_ids(jax.random.fold_in(arg_keys[7], 71), 0)
    router_probs = jnp.clip(jnp.exp(math.log(1.0) - 2.3025851 * jax.random.uniform(arg_keys[3], (TOKENS, K), jnp.float32) ** shard_levels(arg_keys[3], (TOKENS, K), ((0, 512),), -0.2, 0.2)), 0.1, 1.0)
    gate_weight = gaussian(arg_keys[4], (EXPERTS, D, H), D ** -0.5, 0.125, ((0, 16), (1, 32)))
    up_weight = gaussian(arg_keys[5], (EXPERTS, D, H), D ** -0.5, 0.125, ((0, 16), (1, 32)))
    down_weight = gaussian(arg_keys[6], (EXPERTS, H, D), H ** -0.5, 0.21875, ((0, 16), (1, 32)))
    return {"tokens": tokens, "cotangent": cotangent, "expert_ids": expert_ids, "router_probs": router_probs, "gate_weight": gate_weight, "up_weight": up_weight, "down_weight": down_weight}


def swiglu_rows(x_rows, dy_rows, w_gate, w_up, w_down):
    gate_pre = jnp.dot(x_rows, w_gate, preferred_element_type=jnp.float32)
    up_pre = jnp.dot(x_rows, w_up, preferred_element_type=jnp.float32)
    sig_gate = jax.nn.sigmoid(gate_pre)
    active = gate_pre * sig_gate
    hidden = (active * up_pre).astype(jnp.bfloat16)
    output = jnp.dot(hidden, w_down, preferred_element_type=jnp.float32).astype(jnp.bfloat16)
    grad_hidden = jnp.dot(dy_rows, w_down.T, preferred_element_type=jnp.float32)
    grad_gate = (grad_hidden * up_pre * sig_gate * (1.0 + gate_pre * (1.0 - sig_gate))).astype(jnp.bfloat16)
    grad_up = (grad_hidden * active).astype(jnp.bfloat16)
    grad_rows = (jnp.dot(grad_gate, w_gate.T, preferred_element_type=jnp.float32)
                 + jnp.dot(grad_up, w_up.T, preferred_element_type=jnp.float32)).astype(jnp.bfloat16)
    partial_value = jnp.dot(hidden.T, dy_rows, preferred_element_type=jnp.float32).astype(jnp.bfloat16)
    return output, grad_rows, partial_value


def reference(tokens, cotangent, expert_ids, router_probs, gate_weight, up_weight, down_weight):
    group_size = TOK_DEV * EXPERTS
    group_slots = group_size * K
    slot_count = EXPERTS * CAP
    group_x = tokens.reshape(N_DP, group_size, D)
    group_c = cotangent.reshape(N_DP, group_size, D)
    group_ids = expert_ids.reshape(N_DP, group_slots)
    group_p = router_probs.reshape(N_DP, group_size, K)
    positions = jnp.arange(slot_count, dtype=jnp.int32)

    def per_group(summed, inputs):
        rows_x, rows_c, rows_id, rows_p = inputs
        weighted = (rows_p[:, :, None] * rows_c.astype(jnp.float32)[:, None, :]).astype(jnp.bfloat16).reshape(group_slots, D)

        def per_expert(totals, expert):
            out_acc, grad_acc = totals
            chosen = rows_id == expert
            picked = jnp.nonzero(chosen, size=slot_count, fill_value=0)[0].astype(jnp.int32)
            is_live = (positions < jnp.sum(chosen.astype(jnp.int32)))[:, None]
            x_rows = jnp.where(is_live, rows_x[picked // K], jnp.zeros((), jnp.bfloat16))
            dy_rows = jnp.where(is_live, weighted[picked], jnp.zeros((), jnp.bfloat16))
            output, grad_rows, partial_value = swiglu_rows(x_rows, dy_rows, gate_weight[expert], up_weight[expert], down_weight[expert])
            out_acc = out_acc.at[picked].add(jnp.where(is_live, output.astype(jnp.float32), jnp.zeros((), jnp.float32)))
            grad_acc = grad_acc.at[picked].add(jnp.where(is_live, grad_rows.astype(jnp.float32), jnp.zeros((), jnp.float32)))
            return (out_acc, grad_acc), partial_value

        empty_rows = jnp.zeros((group_slots, D), jnp.float32)
        (out_acc, grad_acc), partials = lax.scan(per_expert, (empty_rows, empty_rows), jnp.arange(EXPERTS, dtype=jnp.int32))
        outs = out_acc.reshape(group_size, K, D)
        mixed = jnp.sum(rows_p[:, :, None] * outs, axis=1).astype(jnp.bfloat16)
        probs_grad = jnp.sum(rows_c.astype(jnp.float32)[:, None, :] * outs, axis=2)
        tok_grad = jnp.sum(grad_acc.reshape(group_size, K, D), axis=1).astype(jnp.bfloat16)
        return summed + partials.astype(jnp.float32), (mixed, tok_grad, probs_grad)

    start_sum = jnp.zeros((EXPERTS, H, D), jnp.float32)
    summed, (mixed_all, tok_all, probs_all) = lax.scan(per_group, start_sum, (group_x, group_c, group_ids, group_p))
    mixed_out = mixed_all.reshape(TOKENS, D)
    grad_tokens = tok_all.reshape(TOKENS, D)
    grad_probs = probs_all.reshape(TOKENS, K)
    return mixed_out, grad_tokens, grad_probs, summed.astype(jnp.bfloat16)
```

```python
import jax
import jax.numpy as jnp
from jax import lax
from jax.sharding import PartitionSpec as P


def shards(tokens, cotangent, expert_ids, router_probs, gate_weight, up_weight, down_weight):
    tok_count = tokens.shape[0]
    features = tokens.shape[1]
    choices_each = expert_ids.shape[1]
    slot_total = tok_count * choices_each
    groups = lax.axis_size("expert")
    capacity = 9 * slot_total // (8 * groups)
    slot_count = groups * capacity
    flat_ids = expert_ids.reshape(slot_total)
    member = (flat_ids[:, None] == jnp.arange(groups, dtype=jnp.int32)[None, :]).astype(jnp.int32)
    before = jnp.cumsum(member, axis=0) - member
    target = flat_ids * capacity + jnp.sum(before * member, axis=1)
    placer = (target[None, :] == jnp.arange(slot_count, dtype=jnp.int32)[:, None]).astype(
        jnp.bfloat16
    )
    placer_tok = jnp.sum(placer.reshape(slot_count, tok_count, choices_each), axis=2)
    weighted = (
        (router_probs[:, :, None] * cotangent.astype(jnp.float32)[:, None, :])
        .astype(jnp.bfloat16)
        .reshape(slot_total, features)
    )
    send_rows = jnp.dot(placer_tok, tokens, preferred_element_type=jnp.float32).astype(jnp.bfloat16)
    send_grad = jnp.dot(placer, weighted, preferred_element_type=jnp.float32).astype(jnp.bfloat16)
    recv_both = lax.all_to_all(
        jnp.concatenate([send_rows, send_grad], axis=1).reshape(groups, capacity, 2 * features),
        "expert",
        split_axis=0,
        concat_axis=0,
        tiled=True,
    ).reshape(slot_count, 2 * features)
    x_rows = recv_both[:, :features]
    dy_rows = recv_both[:, features:]
    n_dp = lax.axis_size("dp")
    hidden_units = gate_weight.shape[2]
    rows_dp = down_weight.shape[1]
    stacked = jnp.stack(
        [gate_weight[0], up_weight[0], down_weight[0].reshape(gate_weight.shape[1], hidden_units)]
    )
    all_w = lax.all_gather(stacked[None], "dp", axis=0, tiled=True)
    w_gate = all_w[:, 0].reshape(n_dp * gate_weight.shape[1], hidden_units)
    w_up = all_w[:, 1].reshape(n_dp * gate_weight.shape[1], hidden_units)
    weight_rows = all_w[:, 2].reshape(n_dp * rows_dp, features)
    gate_pre = jnp.dot(x_rows, w_gate, preferred_element_type=jnp.float32)
    up_pre = jnp.dot(x_rows, w_up, preferred_element_type=jnp.float32)
    sig_gate = jax.nn.sigmoid(gate_pre)
    active = gate_pre * sig_gate
    hidden = (active * up_pre).astype(jnp.bfloat16)
    contract = (((1,), (1,)), ((), ()))
    part_hidden = hidden
    acc_part = jnp.dot(part_hidden, weight_rows, preferred_element_type=jnp.float32)
    back_part = lax.dot_general(dy_rows, weight_rows, contract, preferred_element_type=jnp.float32)
    output = acc_part.astype(jnp.bfloat16)
    grad_gate = (back_part * up_pre * sig_gate * (1.0 + gate_pre * (1.0 - sig_gate))).astype(
        jnp.bfloat16
    )
    grad_up = (back_part * active).astype(jnp.bfloat16)
    grad_rows = (
        lax.dot_general(grad_gate, w_gate, contract, preferred_element_type=jnp.float32)
        + lax.dot_general(grad_up, w_up, contract, preferred_element_type=jnp.float32)
    ).astype(jnp.bfloat16)
    back_both = lax.all_to_all(
        jnp.concatenate([output, grad_rows], axis=1).reshape(groups, capacity, 2 * features),
        "expert",
        split_axis=0,
        concat_axis=0,
        tiled=True,
    ).reshape(slot_count, 2 * features)
    back_out = back_both[:, :features]
    back_grad = back_both[:, features:]
    unplace = (((0,), (0,)), ((), ()))
    gathered = lax.dot_general(
        placer, back_out, unplace, preferred_element_type=jnp.float32
    )
    gathered = gathered.reshape(tok_count, choices_each, features)
    grad_tokens = lax.dot_general(
        placer_tok,
        back_grad,
        unplace,
        preferred_element_type=jnp.float32,
    ).astype(jnp.bfloat16)
    mixed_out = jnp.sum(router_probs[:, :, None] * gathered, axis=1).astype(jnp.bfloat16)
    grad_probs = jnp.sum(cotangent.astype(jnp.float32)[:, None, :] * gathered, axis=2)
    part_hidden = hidden
    partial_value = lax.dot_general(
        part_hidden, dy_rows, (((0,), (0,)), ((), ())), preferred_element_type=jnp.float32
    ).astype(jnp.bfloat16)
    grad_down = (
        jnp.sum(
            lax.all_to_all(
                partial_value.reshape(n_dp, rows_dp, features), "dp", 0, 0, tiled=True
            ).astype(jnp.float32),
            axis=0,
        )
        .astype(jnp.bfloat16)[None]
    )
    return (mixed_out, grad_tokens, grad_probs, grad_down)


def solution(mesh):
    placed = (
        P(("dp", "expert"), None),
        P(("dp", "expert"), None),
        P(("dp", "expert"), None),
        P(("dp", "expert"), None),
        P("expert", "dp", None),
        P("expert", "dp", None),
        P("expert", "dp", None),
    )
    return jax.shard_map(
        shards,
        mesh=mesh,
        in_specs=placed,
        out_specs=(
            P(("dp", "expert"), None),
            P(("dp", "expert"), None),
            P(("dp", "expert"), None),
            P("expert", "dp", None),
        ),
        check_vma=False,
    )
```

```python
import jax
import jax.numpy as jnp
from jax import lax
from jax.sharding import Mesh, PartitionSpec as P


def shards(tokens, cotangent, expert_ids, router_probs, gate_weight, up_weight, down_weight):
    tok_count = tokens.shape[0]
    features = tokens.shape[1]
    choices_each = expert_ids.shape[1]
    slot_total = tok_count * choices_each
    groups = lax.axis_size("expert")
    capacity = 9 * slot_total // (8 * groups)
    slot_count = groups * capacity
    flat_ids = expert_ids.reshape(slot_total)
    member = (flat_ids[:, None] == jnp.arange(groups, dtype=jnp.int32)[None, :]).astype(jnp.int32)
    before = jnp.cumsum(member, axis=0) - member
    target = flat_ids * capacity + jnp.sum(before * member, axis=1)
    placer = (target[None, :] == jnp.arange(slot_count, dtype=jnp.int32)[:, None]).astype(
        jnp.bfloat16
    )
    placer_tok = jnp.sum(placer.reshape(slot_count, tok_count, choices_each), axis=2)
    weighted = (
        (router_probs[:, :, None] * cotangent.astype(jnp.float32)[:, None, :])
        .astype(jnp.bfloat16)
        .reshape(slot_total, features)
    )
    send_rows = jnp.dot(placer_tok, tokens, preferred_element_type=jnp.float32).astype(jnp.bfloat16)
    send_grad = jnp.dot(placer, weighted, preferred_element_type=jnp.float32).astype(jnp.bfloat16)
    recv_both = lax.all_to_all(
        jnp.concatenate([send_rows, send_grad], axis=1).reshape(groups, capacity, 2 * features),
        "expert",
        split_axis=0,
        concat_axis=0,
        tiled=True,
    ).reshape(slot_count, 2 * features)
    x_rows = recv_both[:, :features]
    dy_rows = recv_both[:, features:]
    n_dp = lax.axis_size(("dx", "dy"))
    hidden_units = gate_weight.shape[2]
    rows_dp = down_weight.shape[1]
    stacked = jnp.stack(
        [gate_weight[0], up_weight[0], down_weight[0].reshape(gate_weight.shape[1], hidden_units)]
    )
    all_w = lax.all_gather(stacked[None], ("dx", "dy"), axis=0, tiled=True)
    w_gate = all_w[:, 0].reshape(n_dp * gate_weight.shape[1], hidden_units)
    w_up = all_w[:, 1].reshape(n_dp * gate_weight.shape[1], hidden_units)
    weight_rows = all_w[:, 2].reshape(n_dp * rows_dp, features)
    gate_pre = jnp.dot(x_rows, w_gate, preferred_element_type=jnp.float32)
    up_pre = jnp.dot(x_rows, w_up, preferred_element_type=jnp.float32)
    sig_gate = jax.nn.sigmoid(gate_pre)
    active = gate_pre * sig_gate
    hidden = (active * up_pre).astype(jnp.bfloat16)
    contract = (((1,), (1,)), ((), ()))
    part_hidden = hidden
    partial_value = lax.dot_general(
        part_hidden, dy_rows, (((0,), (0,)), ((), ())), preferred_element_type=jnp.float32
    ).astype(jnp.bfloat16)
    acc_part = jnp.dot(part_hidden, weight_rows, preferred_element_type=jnp.float32)
    back_part = lax.dot_general(dy_rows, weight_rows, contract, preferred_element_type=jnp.float32)
    output = acc_part.astype(jnp.bfloat16)
    grad_gate = (back_part * up_pre * sig_gate * (1.0 + gate_pre * (1.0 - sig_gate))).astype(
        jnp.bfloat16
    )
    grad_up = (back_part * active).astype(jnp.bfloat16)
    grad_rows = (
        lax.dot_general(grad_gate, w_gate, contract, preferred_element_type=jnp.float32)
        + lax.dot_general(grad_up, w_up, contract, preferred_element_type=jnp.float32)
    ).astype(jnp.bfloat16)
    back_both = lax.all_to_all(
        jnp.concatenate([output, grad_rows], axis=1).reshape(groups, capacity, 2 * features),
        "expert",
        split_axis=0,
        concat_axis=0,
        tiled=True,
    ).reshape(slot_count, 2 * features)
    back_out = back_both[:, :features]
    back_grad = back_both[:, features:]
    unplace = (((0,), (0,)), ((), ()))
    gathered = lax.dot_general(
        placer, back_out, unplace, preferred_element_type=jnp.float32
    )
    gathered = gathered.reshape(tok_count, choices_each, features)
    grad_tokens = lax.dot_general(
        placer_tok,
        back_grad,
        unplace,
        preferred_element_type=jnp.float32,
    ).astype(jnp.bfloat16)
    mixed_out = jnp.sum(router_probs[:, :, None] * gathered, axis=1).astype(jnp.bfloat16)
    grad_probs = jnp.sum(cotangent.astype(jnp.float32)[:, None, :] * gathered, axis=2)
    grad_down = lax.psum_scatter(
        lax.psum_scatter(partial_value, "dx", scatter_dimension=0, tiled=True),
        "dy",
        scatter_dimension=0,
        tiled=True,
    )[None]
    return (mixed_out, grad_tokens, grad_probs, grad_down)


def solution(mesh):
    n_x = 4
    split = Mesh(
        mesh.devices.reshape(n_x, mesh.shape["dp"] // n_x, mesh.shape["expert"]),
        ("dx", "dy", "expert"),
    )
    rows = P(("dx", "dy", "expert"), None)
    experts = P("expert", ("dx", "dy"), None)
    placed = (rows, rows, rows, rows, experts, experts, experts)
    return jax.shard_map(
        shards,
        mesh=split,
        in_specs=placed,
        out_specs=(rows, rows, rows, experts),
        check_vma=False,
    )
```

```python
import jax
import jax.numpy as jnp
from jax import lax
from jax.sharding import Mesh, PartitionSpec as P


def shards(tokens, cotangent, expert_ids, router_probs, gate_weight, up_weight, down_weight):
    tok_count = tokens.shape[0]
    features = tokens.shape[1]
    choices_each = expert_ids.shape[1]
    slot_total = tok_count * choices_each
    groups = lax.axis_size("expert")
    capacity = 9 * slot_total // (8 * groups)
    slot_count = groups * capacity
    n_dp = lax.axis_size(("dx", "dy"))
    rows_in = gate_weight.shape[1]
    hidden_units = gate_weight.shape[2]
    rows_dp = down_weight.shape[1]
    stacked = jnp.stack(
        [gate_weight[0], up_weight[0], down_weight[0].reshape(rows_in, hidden_units)]
    )
    all_w = lax.all_gather(stacked, ("dx", "dy"), axis=1, tiled=True)
    w_gate = all_w[0]
    w_up = all_w[1]
    weight_rows = all_w[2].reshape(n_dp * rows_dp, features)
    flat_ids = expert_ids.reshape(slot_total)
    member = (flat_ids[:, None] == jnp.arange(groups, dtype=jnp.int32)[None, :]).astype(jnp.int32)
    before = jnp.cumsum(member, axis=0) - member
    target = flat_ids * capacity + jnp.sum(before * member, axis=1)
    target_k = target.reshape(tok_count, choices_each)
    slot_ids = jnp.arange(slot_count, dtype=jnp.int32)[:, None]
    placers = [
        (target_k[None, :, k] == slot_ids).astype(jnp.bfloat16) for k in range(choices_each)
    ]
    placer_tok = sum(placers[1:], placers[0])
    cot32 = cotangent.astype(jnp.float32)
    send_rows = jnp.dot(placer_tok, tokens, preferred_element_type=jnp.float32)
    send_grad = sum(
        jnp.dot(
            placers[k],
            (router_probs[:, k, None] * cot32).astype(jnp.bfloat16),
            preferred_element_type=jnp.float32,
        )
        for k in range(choices_each)
    )
    recv_both = lax.all_to_all(
        jnp.concatenate([send_rows, send_grad], axis=1).astype(jnp.bfloat16),
        "expert",
        split_axis=0,
        concat_axis=0,
        tiled=True,
    )
    x_rows = recv_both[:, :features]
    dy_rows = recv_both[:, features:]
    gate_pre = jnp.dot(x_rows, w_gate, preferred_element_type=jnp.float32)
    up_pre = jnp.dot(x_rows, w_up, preferred_element_type=jnp.float32)
    sig_gate = jax.nn.sigmoid(gate_pre)
    active = gate_pre * sig_gate
    hidden = (active * up_pre).astype(jnp.bfloat16)
    contract = (((1,), (1,)), ((), ()))
    partial_value = lax.dot_general(
        hidden, dy_rows, (((0,), (0,)), ((), ())), preferred_element_type=jnp.float32
    ).astype(jnp.bfloat16)
    output = jnp.dot(hidden, weight_rows, preferred_element_type=jnp.float32).astype(jnp.bfloat16)
    back_out = lax.all_to_all(output, "expert", split_axis=0, concat_axis=0, tiled=True)
    back_part = lax.dot_general(dy_rows, weight_rows, contract, preferred_element_type=jnp.float32)
    grad_gate = (back_part * up_pre * sig_gate * (1.0 + gate_pre * (1.0 - sig_gate))).astype(
        jnp.bfloat16
    )
    grad_up = (back_part * active).astype(jnp.bfloat16)
    grad_rows = (
        lax.dot_general(grad_gate, w_gate, contract, preferred_element_type=jnp.float32)
        + lax.dot_general(grad_up, w_up, contract, preferred_element_type=jnp.float32)
    ).astype(jnp.bfloat16)
    back_grad = lax.all_to_all(grad_rows, "expert", split_axis=0, concat_axis=0, tiled=True)
    unplace = (((0,), (0,)), ((), ()))
    gathered = [
        lax.dot_general(placers[k], back_out, unplace, preferred_element_type=jnp.float32)
        for k in range(choices_each)
    ]
    mixed_out = sum(
        router_probs[:, k, None] * gathered[k] for k in range(choices_each)
    ).astype(jnp.bfloat16)
    grad_probs = jnp.stack(
        [jnp.sum(cot32 * gathered[k], axis=1) for k in range(choices_each)], axis=1
    )
    grad_tokens = lax.dot_general(
        placer_tok, back_grad, unplace, preferred_element_type=jnp.float32
    ).astype(jnp.bfloat16)
    grad_down = lax.psum_scatter(
        lax.psum_scatter(partial_value, "dx", scatter_dimension=0, tiled=True),
        "dy",
        scatter_dimension=0,
        tiled=True,
    )[None]
    return (mixed_out, grad_tokens, grad_probs, grad_down)


def solution(mesh):
    n_x = 4
    split = Mesh(
        mesh.devices.reshape(n_x, mesh.shape["dp"] // n_x, mesh.shape["expert"]),
        ("dx", "dy", "expert"),
    )
    rows = P(("dx", "dy", "expert"), None)
    experts = P("expert", ("dx", "dy"), None)
    placed = (rows, rows, rows, rows, experts, experts, experts)
    return jax.shard_map(
        shards,
        mesh=split,
        in_specs=placed,
        out_specs=(rows, rows, rows, experts),
        check_vma=False,
    )
```

```python
import jax
import jax.numpy as jnp
from jax import lax
from jax.sharding import Mesh, PartitionSpec as P


def shards(tokens, cotangent, expert_ids, router_probs, gate_weight, up_weight, down_weight):
    tok_count = tokens.shape[0]
    features = tokens.shape[1]
    choices_each = expert_ids.shape[1]
    slot_total = tok_count * choices_each
    groups = lax.axis_size("expert")
    capacity = 9 * slot_total // (8 * groups)
    slot_count = groups * capacity
    n_dp = lax.axis_size(("dx", "dy"))
    rows_in = gate_weight.shape[1]
    hidden_units = gate_weight.shape[2]
    rows_dp = down_weight.shape[1]
    stacked = jnp.stack(
        [gate_weight[0], up_weight[0], down_weight[0].reshape(rows_in, hidden_units)]
    )
    all_w = lax.all_gather(stacked, ("dx", "dy"), axis=1, tiled=True)
    w_gate = all_w[0]
    w_up = all_w[1]
    weight_rows = all_w[2].reshape(n_dp * rows_dp, features)
    flat_ids = expert_ids.reshape(slot_total)
    member = (flat_ids[:, None] == jnp.arange(groups, dtype=jnp.int32)[None, :]).astype(jnp.int32)
    before = jnp.cumsum(member, axis=0) - member
    target = flat_ids * capacity + jnp.sum(before * member, axis=1)
    target_k = target.reshape(tok_count, choices_each)
    slot_ids = jnp.arange(slot_count, dtype=jnp.int32)[:, None]
    placers = [
        (target_k[None, :, k] == slot_ids).astype(jnp.bfloat16) for k in range(choices_each)
    ]
    placer_tok = sum(placers[1:], placers[0])
    cot32 = cotangent.astype(jnp.float32)
    send_rows = jnp.dot(placer_tok, tokens, preferred_element_type=jnp.float32)
    send_grad = sum(
        jnp.dot(
            placers[k],
            (router_probs[:, k, None] * cot32).astype(jnp.bfloat16),
            preferred_element_type=jnp.float32,
        )
        for k in range(choices_each)
    )
    recv_both = lax.all_to_all(
        jnp.concatenate([send_rows, send_grad], axis=1).astype(jnp.bfloat16),
        "expert",
        split_axis=0,
        concat_axis=0,
        tiled=True,
    )
    x_rows = recv_both[:, :features]
    dy_rows = recv_both[:, features:]
    gate_pre = jnp.dot(x_rows, w_gate, preferred_element_type=jnp.float32)
    up_pre = jnp.dot(x_rows, w_up, preferred_element_type=jnp.float32)
    sig_gate = jax.nn.sigmoid(gate_pre)
    active = gate_pre * sig_gate
    hidden = (active * up_pre).astype(jnp.bfloat16)
    contract = (((1,), (1,)), ((), ()))
    partial_value = lax.dot_general(
        hidden, dy_rows, (((0,), (0,)), ((), ())), preferred_element_type=jnp.float32
    ).astype(jnp.bfloat16)
    output = jnp.dot(hidden, weight_rows, preferred_element_type=jnp.float32).astype(jnp.bfloat16)
    back_out = lax.all_to_all(
        output.reshape(groups, capacity, features), "expert", split_axis=0, concat_axis=0, tiled=True
    )
    back_part = lax.dot_general(dy_rows, weight_rows, contract, preferred_element_type=jnp.float32)
    grad_gate = (back_part * up_pre * sig_gate * (1.0 + gate_pre * (1.0 - sig_gate))).astype(
        jnp.bfloat16
    )
    grad_up = (back_part * active).astype(jnp.bfloat16)
    grad_rows = (
        lax.dot_general(grad_gate, w_gate, contract, preferred_element_type=jnp.float32)
        + lax.dot_general(grad_up, w_up, contract, preferred_element_type=jnp.float32)
    ).astype(jnp.bfloat16)
    back_grad = lax.all_to_all(
        grad_rows.reshape(groups, capacity, features), "expert", split_axis=0, concat_axis=0, tiled=True
    )
    unplace = (((0, 1), (0, 1)), ((), ()))
    placers = [p.reshape(groups, capacity, tok_count) for p in placers]
    placer_tok = placer_tok.reshape(groups, capacity, tok_count)
    gathered = [
        lax.dot_general(placers[k], back_out, unplace, preferred_element_type=jnp.float32)
        for k in range(choices_each)
    ]
    mixed_out = sum(
        router_probs[:, k, None] * gathered[k] for k in range(choices_each)
    ).astype(jnp.bfloat16)
    grad_probs = jnp.stack(
        [jnp.sum(cot32 * gathered[k], axis=1) for k in range(choices_each)], axis=1
    )
    grad_tokens = lax.dot_general(
        placer_tok, back_grad, unplace, preferred_element_type=jnp.float32
    ).astype(jnp.bfloat16)
    grad_down = lax.psum_scatter(
        lax.psum_scatter(partial_value, "dx", scatter_dimension=0, tiled=True),
        "dy",
        scatter_dimension=0,
        tiled=True,
    )[None]
    return (mixed_out, grad_tokens, grad_probs, grad_down)


def solution(mesh):
    n_x = 4
    split = Mesh(
        mesh.devices.reshape(n_x, mesh.shape["dp"] // n_x, mesh.shape["expert"]),
        ("dx", "dy", "expert"),
    )
    rows = P(("dx", "dy", "expert"), None)
    experts = P("expert", ("dx", "dy"), None)
    placed = (rows, rows, rows, rows, experts, experts, experts)
    return jax.shard_map(
        shards,
        mesh=split,
        in_specs=placed,
        out_specs=(rows, rows, rows, experts),
        check_vma=False,
    )
```

```python
import jax
import jax.numpy as jnp
from jax import lax
from jax.sharding import Mesh, PartitionSpec as P


def shards(tokens, cotangent, expert_ids, router_probs, gate_weight, up_weight, down_weight):
    tok_count = tokens.shape[0]
    features = tokens.shape[1]
    choices_each = expert_ids.shape[1]
    slot_total = tok_count * choices_each
    groups = lax.axis_size("expert")
    capacity = 9 * slot_total // (8 * groups)
    slot_count = groups * capacity
    n_dp = lax.axis_size(("dx", "dy"))
    rows_in = gate_weight.shape[1]
    hidden_units = gate_weight.shape[2]
    rows_dp = down_weight.shape[1]
    stacked = jnp.concatenate(
        [gate_weight[0], up_weight[0], down_weight[0].reshape(rows_in, hidden_units)], axis=1
    )
    all_w = lax.all_gather(stacked, ("dx", "dy"), axis=0, tiled=True)
    w_both = all_w[:, : 2 * hidden_units]
    weight_rows = all_w[:, 2 * hidden_units :].reshape(n_dp * rows_dp, features)
    flat_ids = expert_ids.reshape(slot_total)
    member = (flat_ids[:, None] == jnp.arange(groups, dtype=jnp.int32)[None, :]).astype(jnp.int32)
    before = jnp.cumsum(member, axis=0) - member
    target = flat_ids * capacity + jnp.sum(before * member, axis=1)
    target_k = target.reshape(tok_count, choices_each)
    slot_ids = jnp.arange(slot_count, dtype=jnp.int32)[:, None]
    placers = [
        (target_k[None, :, k] == slot_ids).astype(jnp.bfloat16) for k in range(choices_each)
    ]
    placer_tok = sum(placers[1:], placers[0])
    cot32 = cotangent.astype(jnp.float32)
    send_rows = jnp.dot(placer_tok, tokens, preferred_element_type=jnp.float32)
    send_grad = sum(
        jnp.dot(
            placers[k],
            (router_probs[:, k, None] * cot32).astype(jnp.bfloat16),
            preferred_element_type=jnp.float32,
        )
        for k in range(choices_each)
    )
    recv_both = lax.all_to_all(
        jnp.concatenate([send_rows, send_grad], axis=1).astype(jnp.bfloat16),
        "expert",
        split_axis=0,
        concat_axis=0,
        tiled=True,
    )
    x_rows = recv_both[:, :features]
    dy_rows = recv_both[:, features:]
    both_pre = jnp.dot(x_rows, w_both, preferred_element_type=jnp.float32)
    gate_pre = both_pre[:, :hidden_units]
    up_pre = both_pre[:, hidden_units:]
    sig_gate = jax.nn.sigmoid(gate_pre)
    active = gate_pre * sig_gate
    hidden = (active * up_pre).astype(jnp.bfloat16)
    contract = (((1,), (1,)), ((), ()))
    partial_value = lax.dot_general(
        hidden, dy_rows, (((0,), (0,)), ((), ())), preferred_element_type=jnp.float32
    ).astype(jnp.bfloat16)
    output = jnp.dot(hidden, weight_rows, preferred_element_type=jnp.float32).astype(jnp.bfloat16)
    back_out = lax.all_to_all(
        output.reshape(groups, capacity, features), "expert", split_axis=0, concat_axis=0, tiled=True
    )
    back_part = lax.dot_general(dy_rows, weight_rows, contract, preferred_element_type=jnp.float32)
    grad_gate = (back_part * up_pre * sig_gate * (1.0 + gate_pre * (1.0 - sig_gate))).astype(
        jnp.bfloat16
    )
    grad_up = (back_part * active).astype(jnp.bfloat16)
    grad_rows = lax.dot_general(
        jnp.concatenate([grad_gate, grad_up], axis=1),
        w_both,
        contract,
        preferred_element_type=jnp.float32,
    ).astype(jnp.bfloat16)
    back_grad = lax.all_to_all(
        grad_rows.reshape(groups, capacity, features), "expert", split_axis=0, concat_axis=0, tiled=True
    )
    unplace = (((0, 1), (0, 1)), ((), ()))
    placers = [p.reshape(groups, capacity, tok_count) for p in placers]
    placer_tok = placer_tok.reshape(groups, capacity, tok_count)
    gathered = [
        lax.dot_general(placers[k], back_out, unplace, preferred_element_type=jnp.float32)
        for k in range(choices_each)
    ]
    mixed_out = sum(
        router_probs[:, k, None] * gathered[k] for k in range(choices_each)
    ).astype(jnp.bfloat16)
    grad_probs = jnp.stack(
        [jnp.sum(cot32 * gathered[k], axis=1) for k in range(choices_each)], axis=1
    )
    grad_tokens = lax.dot_general(
        placer_tok, back_grad, unplace, preferred_element_type=jnp.float32
    ).astype(jnp.bfloat16)
    grad_down = lax.psum_scatter(
        lax.psum_scatter(partial_value, "dx", scatter_dimension=0, tiled=True),
        "dy",
        scatter_dimension=0,
        tiled=True,
    )[None]
    return (mixed_out, grad_tokens, grad_probs, grad_down)


def solution(mesh):
    n_x = 4
    split = Mesh(
        mesh.devices.reshape(n_x, mesh.shape["dp"] // n_x, mesh.shape["expert"]),
        ("dx", "dy", "expert"),
    )
    rows = P(("dx", "dy", "expert"), None)
    experts = P("expert", ("dx", "dy"), None)
    placed = (rows, rows, rows, rows, experts, experts, experts)
    return jax.shard_map(
        shards,
        mesh=split,
        in_specs=placed,
        out_specs=(rows, rows, rows, experts),
        check_vma=False,
    )
```

```python
import jax
import jax.numpy as jnp
from jax import lax
from jax.sharding import Mesh, PartitionSpec as P


def shards(tokens, cotangent, expert_ids, router_probs, gate_weight, up_weight, down_weight):
    tok_count = tokens.shape[0]
    features = tokens.shape[1]
    choices_each = expert_ids.shape[1]
    slot_total = tok_count * choices_each
    groups = lax.axis_size("expert")
    capacity = 9 * slot_total // (8 * groups)
    slot_count = groups * capacity
    n_dp = lax.axis_size(("dx", "dy"))
    rows_in = gate_weight.shape[1]
    hidden_units = gate_weight.shape[2]
    rows_dp = down_weight.shape[1]
    stacked = jnp.concatenate(
        [gate_weight[0], up_weight[0], down_weight[0].reshape(rows_in, hidden_units)], axis=1
    )
    all_w = lax.all_gather(stacked, ("dx", "dy"), axis=0, tiled=True)
    w_both = all_w[:, : 2 * hidden_units]
    weight_rows = all_w[:, 2 * hidden_units :].reshape(n_dp * rows_dp, features)
    flat_ids = expert_ids.reshape(slot_total)
    member = (flat_ids[:, None] == jnp.arange(groups, dtype=jnp.int32)[None, :]).astype(jnp.int32)
    before = jnp.cumsum(member, axis=0) - member
    target = flat_ids * capacity + jnp.sum(before * member, axis=1)
    target_k = target.reshape(tok_count, choices_each)
    slot_ids = jnp.arange(slot_count, dtype=jnp.int32)[:, None]
    placers = [
        (target_k[None, :, k] == slot_ids).astype(jnp.bfloat16) for k in range(choices_each)
    ]
    placer_tok = sum(placers[1:], placers[0])
    cot32 = cotangent.astype(jnp.float32)
    send_rows = jnp.dot(placer_tok, tokens, preferred_element_type=jnp.float32)
    send_grad = sum(
        jnp.dot(
            placers[k],
            (router_probs[:, k, None] * cot32).astype(jnp.bfloat16),
            preferred_element_type=jnp.float32,
        )
        for k in range(choices_each)
    )
    recv_both = lax.all_to_all(
        jnp.concatenate([send_rows, send_grad], axis=1).astype(jnp.bfloat16),
        "expert",
        split_axis=0,
        concat_axis=0,
        tiled=True,
    )
    x_rows = recv_both[:, :features]
    dy_rows = recv_both[:, features:]
    both_pre = jnp.dot(x_rows, w_both, preferred_element_type=jnp.float32)
    gate_pre = both_pre[:, :hidden_units]
    up_pre = both_pre[:, hidden_units:]
    sig_gate = jax.nn.sigmoid(gate_pre)
    active = gate_pre * sig_gate
    hidden = (active * up_pre).astype(jnp.bfloat16)
    contract = (((1,), (1,)), ((), ()))
    n_x = lax.axis_size("dx")
    n_y = lax.axis_size("dy")
    hidden_yx = (
        hidden.reshape(slot_count, n_x, n_y, rows_dp)
        .transpose(0, 2, 1, 3)
        .reshape(slot_count, n_dp * rows_dp)
    )
    partial_value = lax.dot_general(
        hidden_yx, dy_rows, (((0,), (0,)), ((), ())), preferred_element_type=jnp.float32
    ).astype(jnp.bfloat16)
    output = jnp.dot(hidden, weight_rows, preferred_element_type=jnp.float32).astype(jnp.bfloat16)
    back_out = lax.all_to_all(
        output.reshape(groups, capacity, features), "expert", split_axis=0, concat_axis=0, tiled=True
    )
    back_part = lax.dot_general(dy_rows, weight_rows, contract, preferred_element_type=jnp.float32)
    grad_gate = (back_part * up_pre * sig_gate * (1.0 + gate_pre * (1.0 - sig_gate))).astype(
        jnp.bfloat16
    )
    grad_up = (back_part * active).astype(jnp.bfloat16)
    grad_rows = lax.dot_general(
        jnp.concatenate([grad_gate, grad_up], axis=1),
        w_both,
        contract,
        preferred_element_type=jnp.float32,
    ).astype(jnp.bfloat16)
    back_grad = lax.all_to_all(
        grad_rows.reshape(groups, capacity, features), "expert", split_axis=0, concat_axis=0, tiled=True
    )
    unplace = (((0, 1), (0, 1)), ((), ()))
    placers = [p.reshape(groups, capacity, tok_count) for p in placers]
    placer_tok = placer_tok.reshape(groups, capacity, tok_count)
    gathered = [
        lax.dot_general(placers[k], back_out, unplace, preferred_element_type=jnp.float32)
        for k in range(choices_each)
    ]
    mixed_out = sum(
        router_probs[:, k, None] * gathered[k] for k in range(choices_each)
    ).astype(jnp.bfloat16)
    grad_probs = jnp.stack(
        [jnp.sum(cot32 * gathered[k], axis=1) for k in range(choices_each)], axis=1
    )
    grad_tokens = lax.dot_general(
        placer_tok, back_grad, unplace, preferred_element_type=jnp.float32
    ).astype(jnp.bfloat16)
    grad_down = lax.psum_scatter(
        lax.psum_scatter(partial_value, "dy", scatter_dimension=0, tiled=True),
        "dx",
        scatter_dimension=0,
        tiled=True,
    )[None]
    return (mixed_out, grad_tokens, grad_probs, grad_down)


def solution(mesh):
    n_x = 4
    split = Mesh(
        mesh.devices.reshape(n_x, mesh.shape["dp"] // n_x, mesh.shape["expert"]),
        ("dx", "dy", "expert"),
    )
    rows = P(("dx", "dy", "expert"), None)
    experts = P("expert", ("dx", "dy"), None)
    placed = (rows, rows, rows, rows, experts, experts, experts)
    return jax.shard_map(
        shards,
        mesh=split,
        in_specs=placed,
        out_specs=(rows, rows, rows, experts),
        check_vma=False,
    )
```
